32 devices in a mesh: row: 4 (over y, core), col: 8 (over z, x).
Axes of the slice: x: 2, y: 2, z: 4, core: 2. Of those that a mesh axis runs over, the one named last changes fastest.
Arguments:
- tokens: bfloat16 [1024, 16384], P('col', 'row'), may hold values from -6 to 6
- gate_weight: bfloat16 [16384, 26624], P('row', 'col'), may hold values from -0.046875 to 0.046875
- up_weight: bfloat16 [16384, 26624], P('row', 'col'), may hold values from -0.046875 to 0.046875
Outputs:
- hidden: bfloat16 [1024, 26624], P('row', 'col')
The draws below stay inside these ranges and needn't reach their ends.
All inputs are finite; a program needn't handle non-finite values.
Results may differ from the reference program's by a relative error of at most 0.02.
Values may be sent and summed in bfloat16 or wider, within the bound.
No kernel may reach another device: no remote copies, remote signals or barrier semaphores. Data moves between devices by JAX's collectives and lax.ppermute only.
A program may use at most 192 MiB of HBM per device.

```python
import jax
import jax.numpy as jnp
from jax import lax

D = 16384
FFW = 26624
TOKENS = 1024
KBLOCK = 4096
N_ROW = 4


def strengthened(array, key, source, target, shards_of, factor):
    def block_of(axis_at):
        return (jnp.arange(array.shape[axis_at]) // (array.shape[axis_at] // shards_of)).reshape((-1,) + (1,) * (array.ndim - 1 - axis_at))

    one_side = jax.random.permutation(key, shards_of)[block_of(target)]
    far = (block_of(target) + shards_of // 2) % shards_of
    return jnp.where((block_of(source) == one_side) | (block_of(source) == far), factor * array, array)


def shard_levels(rng, dims, split, least, high):
    loudness, own = 1.0, jax.random.fold_in(rng, 6)
    for dim, parts in split:
        draws = jnp.exp(jax.random.uniform(jax.random.fold_in(own, dim), (parts,), jnp.float32, least / len(split), high / len(split)))
        loudness = loudness * jnp.repeat(draws, dims[dim] // parts).reshape([-1 if axis == dim else 1 for axis in range(len(dims))])
    return loudness


def bell_draw(key, dims, spread, limit, split=(), held_as=jnp.bfloat16):
    result = spread * jax.random.normal(key, dims, jnp.float32)
    if split:
        result = result * shard_levels(key, dims, split, -0.22, 0.18)
    return jnp.clip(result, -limit, limit).astype(held_as)


def bell_draw_with(key, dims, width, limit, shards, heavy, kind=jnp.bfloat16):
    result = width * jax.random.normal(key, dims, jnp.float32)
    if shards:
        result = result * shard_levels(key, dims, shards, -0.22, 0.18)
    return jnp.clip(strengthened(result, jax.random.fold_in(key, 3), *heavy), -limit, limit).astype(kind)


def setup_inputs(seed: int = 0) -> dict:
    arg_keys = jax.random.split(jax.random.key(seed), 4)
    tokens = bell_draw_with(arg_keys[0], (TOKENS, D), 1.0, 6.0, ((0, 8), (1, 4)), (1, 0, 8, 2.0))
    gate_weight = bell_draw(arg_keys[1], (D, FFW), D ** -0.5, 0.046875, ((0, 4), (1, 8)))
    up_weight = bell_draw(arg_keys[2], (D, FFW), D ** -0.5, 0.046875, ((0, 4), (1, 8)))
    return dict(tokens=tokens, gate_weight=gate_weight, up_weight=up_weight)


def reference(tokens, gate_weight, up_weight):
    token_blocks = tokens.reshape(TOKENS, N_ROW, KBLOCK).transpose(1, 0, 2)
    gate_blocks = gate_weight.reshape(N_ROW, KBLOCK, FFW)
    up_blocks = up_weight.reshape(N_ROW, KBLOCK, FFW)

    def accumulate(carry, block):
        xs, gw, uw = block
        gate_part = jnp.dot(xs, gw, preferred_element_type=jnp.float32).astype(jnp.bfloat16)
        up_part = jnp.dot(xs, uw, preferred_element_type=jnp.float32).astype(jnp.bfloat16)
        gate_part, up_part = lax.optimization_barrier((gate_part, up_part))
        return (carry[0] + gate_part.astype(jnp.float32), carry[1] + up_part.astype(jnp.float32)), None

    start = (jnp.zeros((TOKENS, FFW), jnp.float32), jnp.zeros((TOKENS, FFW), jnp.float32))
    (gate, up), _ = lax.scan(accumulate, start, (token_blocks, gate_blocks, up_blocks))
    return (jax.nn.silu(gate) * up).astype(jnp.bfloat16)
```

```python
import jax
import jax.numpy as jnp
from jax import lax
from jax.sharding import PartitionSpec as P

CHUNKS = 4


def reduce_rows(part, n_row):
    r = lax.axis_index("row")
    cur = part
    d = 1
    while d < n_row:
        m = cur.shape[0] // (n_row // d)
        x4 = cur.reshape(n_row // (2 * d), 2, m, cur.shape[1])
        bit = (r // d) % 2
        keep = lax.dynamic_index_in_dim(x4, bit, axis=1, keepdims=False)
        send = lax.dynamic_index_in_dim(x4, 1 - bit, axis=1, keepdims=False)
        got = lax.ppermute(
            send.astype(jnp.bfloat16), "row", [(i, i ^ d) for i in range(n_row)]
        )
        cur = (keep.astype(jnp.float32) + got.astype(jnp.float32)).reshape(-1, cur.shape[1])
        d *= 2
    return cur


def make_on_device(n_row, n_col):
    def on_device(tokens, gate_weight, up_weight):
        local = tokens.shape[0]
        tc = local // CHUNKS
        group = n_col // n_row
        gates, ups = [], []
        for i in range(CHUNKS):
            piece = lax.all_gather(tokens[i * tc:(i + 1) * tc], "col", axis=0, tiled=True)
            g = jnp.dot(piece, gate_weight, preferred_element_type=jnp.float32).astype(jnp.bfloat16)
            u = jnp.dot(piece, up_weight, preferred_element_type=jnp.float32).astype(jnp.bfloat16)
            gates.append(reduce_rows(g, n_row))
            ups.append(reduce_rows(u, n_row))
        units = gate_weight.shape[1]

        def assemble(parts):
            x = jnp.stack(parts).reshape(CHUNKS, group, tc, units)
            return x.transpose(1, 0, 2, 3).reshape(group * CHUNKS * tc, units)

        gate = assemble(gates)
        up = assemble(ups)
        return (jax.nn.silu(gate) * up).astype(jnp.bfloat16)

    return on_device


def solution(mesh):
    placed = (P("col", "row"), P("row", "col"), P("row", "col"))
    fn = make_on_device(mesh.shape["row"], mesh.shape["col"])
    return jax.shard_map(
        fn, mesh=mesh, in_specs=placed, out_specs=P("row", "col"), check_vma=False
    )
```

```python
import jax
import jax.numpy as jnp
import numpy as np
from jax import lax
from jax.sharding import PartitionSpec as P

HALVES = 2
SPLIT_UNITS = 2


def ring_order(mesh):
    col = mesh.devices[0]
    n = len(col)
    try:
        zs = sorted({d.coords[2] for d in col})
        xs = sorted({d.coords[0] for d in col})
        at = {(zs.index(d.coords[2]), xs.index(d.coords[0])): i for i, d in enumerate(col)}
    except Exception:
        return list(range(n))
    a, b = len(zs), len(xs)
    if a * b != n or len(at) != n or a % 2 or b < 2:
        return list(range(n))
    cells = [(z, 0) for z in range(a)]
    for k, z in enumerate(range(a - 1, -1, -1)):
        span = range(1, b) if k % 2 == 0 else range(b - 1, 0, -1)
        cells += [(z, x) for x in span]
    return [at[c] for c in cells]


class Ring:
    def __init__(self, order):
        self.order = order
        n = len(order)
        self.n = n
        pos = np.zeros(n, np.int32)
        for q, c in enumerate(order):
            pos[c] = q
        self.pos = pos
        self.fwd_pairs = [(order[q], order[(q + 1) % n]) for q in range(n)]
        self.bwd_pairs = [(order[q], order[(q - 1) % n]) for q in range(n)]
        self.steps = n // 2
        self.back_steps = n - 1 - n // 2

    def init(self, x):
        n = self.n
        c = lax.axis_index("col")
        buf = jnp.zeros((n,) + x.shape, x.dtype)
        buf = lax.dynamic_update_slice(buf, x[None], (c, 0, 0))
        return {"buf": buf, "f": x, "b": x}

    def step(self, st, s):
        n = self.n
        c = lax.axis_index("col")
        p = jnp.asarray(self.pos)[c]
        order_t = jnp.asarray(np.array(self.order, np.int32))
        buf = st["buf"]
        f = lax.ppermute(st["f"], "col", self.fwd_pairs)
        buf = lax.dynamic_update_slice(buf, f[None], (order_t[(p - s) % n], 0, 0))
        b = st["b"]
        if s <= self.back_steps:
            b = lax.ppermute(b, "col", self.bwd_pairs)
            buf = lax.dynamic_update_slice(buf, b[None], (order_t[(p + s) % n], 0, 0))
        return {"buf": buf, "f": f, "b": b}

    def result(self, st):
        buf = st["buf"]
        return buf.reshape((-1,) + buf.shape[2:])


def reduce_level(cur, d, n_row):
    r = lax.axis_index("row")
    m = cur.shape[0] // (n_row // d)
    x4 = cur.reshape(n_row // (2 * d), 2, m, cur.shape[1])
    bit = (r // d) % 2
    keep = lax.dynamic_index_in_dim(x4, bit, axis=1, keepdims=False)
    send = lax.dynamic_index_in_dim(x4, 1 - bit, axis=1, keepdims=False)
    got = lax.ppermute(send.astype(jnp.bfloat16), "row", [(i, i ^ d) for i in range(n_row)])
    return (keep.astype(jnp.float32) + got.astype(jnp.float32)).reshape(-1, cur.shape[1])


def make_on_device(n_row, n_col, order):
    ring = Ring(order)
    levels = []
    d = 1
    while d < n_row:
        levels.append(d)
        d *= 2

    def on_device(tokens, gate_weight, up_weight):
        local = tokens.shape[0]
        tc = local // HALVES
        group = n_col // n_row
        units = gate_weight.shape[1]
        us = units // SPLIT_UNITS

        st = ring.init(tokens[:tc])
        for s in range(1, ring.steps + 1):
            st = ring.step(st, s)
        piece = ring.result(st)

        tiles = []
        for h in range(HALVES):
            for w in range(2):
                for j in range(SPLIT_UNITS):
                    tiles.append((h, w, j))

        jobs = []
        done = {}
        nxt = None
        t = 0
        while t < len(tiles) or jobs:
            carry = {}
            for job in jobs:
                job[2] = reduce_level(job[2], levels[job[1]], n_row)
                job[1] += 1
            if t < len(tiles):
                h, w, j = tiles[t]
                first_of_share = t % (2 * SPLIT_UNITS) == 0
                if first_of_share and h + 1 < HALVES:
                    nxt = {"st": ring.init(tokens[(h + 1) * tc:(h + 2) * tc]), "s": 1}
                if nxt is not None and nxt["s"] <= ring.steps:
                    nxt["st"] = ring.step(nxt["st"], nxt["s"])
                    nxt["s"] += 1
                weight = gate_weight if w == 0 else up_weight
                out = jnp.dot(
                    piece, weight[:, j * us:(j + 1) * us], preferred_element_type=jnp.float32
                ).astype(jnp.bfloat16)
                new_job = [t, 0, out]
            else:
                new_job = None
            finished = [jb for jb in jobs if jb[1] == len(levels)]
            jobs = [jb for jb in jobs if jb[1] < len(levels)]
            for jb in finished:
                done[jb[0]] = jb[2]
            if new_job is not None:
                if levels:
                    jobs.append(new_job)
                else:
                    done[new_job[0]] = new_job[2].astype(jnp.float32)
            carry["piece"] = piece
            carry["jobs"] = [jb[2] for jb in jobs]
            carry["nxt"] = nxt["st"] if nxt is not None else None
            carry["done"] = done
            carry = lax.optimization_barrier(carry)
            piece = carry["piece"]
            for jb, a in zip(jobs, carry["jobs"]):
                jb[2] = a
            if nxt is not None:
                nxt["st"] = carry["nxt"]
            done = carry["done"]
            t += 1
            if t < len(tiles) and t % (2 * SPLIT_UNITS) == 0 and nxt is not None:
                while nxt["s"] <= ring.steps:
                    nxt["st"] = ring.step(nxt["st"], nxt["s"])
                    nxt["s"] += 1
                piece = ring.result(nxt["st"])
                nxt = None

        def assemble(w):
            parts = []
            for h in range(HALVES):
                base = (h * 2 + w) * SPLIT_UNITS
                parts.append(jnp.concatenate([done[base + j] for j in range(SPLIT_UNITS)], axis=1))
            x = jnp.stack(parts).reshape(HALVES, group, tc, units)
            return x.transpose(1, 0, 2, 3).reshape(group * HALVES * tc, units)

        gate = assemble(0)
        up = assemble(1)
        return (jax.nn.silu(gate) * up).astype(jnp.bfloat16)

    return on_device


def solution(mesh):
    placed = (P("col", "row"), P("row", "col"), P("row", "col"))
    fn = make_on_device(mesh.shape["row"], mesh.shape["col"], ring_order(mesh))
    return jax.shard_map(
        fn, mesh=mesh, in_specs=placed, out_specs=P("row", "col"), check_vma=False
    )
```

```python
import jax
import jax.numpy as jnp
import numpy as np
from jax import lax
from jax.sharding import PartitionSpec as P

SPLIT_UNITS = 2


def share_sizes(local):
    first = local // 4
    second = (local - first) // 2
    return [first, second, local - first - second]


def ring_order(mesh):
    col = mesh.devices[0]
    n = len(col)
    try:
        zs = sorted({d.coords[2] for d in col})
        xs = sorted({d.coords[0] for d in col})
        at = {(zs.index(d.coords[2]), xs.index(d.coords[0])): i for i, d in enumerate(col)}
    except Exception:
        return list(range(n))
    a, b = len(zs), len(xs)
    if a * b != n or len(at) != n or a % 2 or b < 2:
        return list(range(n))
    cells = [(z, 0) for z in range(a)]
    for k, z in enumerate(range(a - 1, -1, -1)):
        span = range(1, b) if k % 2 == 0 else range(b - 1, 0, -1)
        cells += [(z, x) for x in span]
    return [at[c] for c in cells]


class Ring:
    def __init__(self, order):
        self.order = order
        n = len(order)
        self.n = n
        pos = np.zeros(n, np.int32)
        for q, c in enumerate(order):
            pos[c] = q
        self.pos = pos
        self.fwd_pairs = [(order[q], order[(q + 1) % n]) for q in range(n)]
        self.bwd_pairs = [(order[q], order[(q - 1) % n]) for q in range(n)]
        self.steps = n // 2
        self.back_steps = n - 1 - n // 2

    def init(self, x):
        n = self.n
        c = lax.axis_index("col")
        buf = jnp.zeros((n,) + x.shape, x.dtype)
        buf = lax.dynamic_update_slice(buf, x[None], (c, 0, 0))
        return {"buf": buf, "f": x, "b": x}

    def step(self, st, s):
        n = self.n
        c = lax.axis_index("col")
        p = jnp.asarray(self.pos)[c]
        order_t = jnp.asarray(np.array(self.order, np.int32))
        buf = st["buf"]
        f = lax.ppermute(st["f"], "col", self.fwd_pairs)
        buf = lax.dynamic_update_slice(buf, f[None], (order_t[(p - s) % n], 0, 0))
        b = st["b"]
        if s <= self.back_steps:
            b = lax.ppermute(b, "col", self.bwd_pairs)
            buf = lax.dynamic_update_slice(buf, b[None], (order_t[(p + s) % n], 0, 0))
        return {"buf": buf, "f": f, "b": b}

    def result(self, st):
        buf = st["buf"]
        return buf.reshape((-1,) + buf.shape[2:])


def reduce_level(cur, d, n_row):
    r = lax.axis_index("row")
    m = cur.shape[0] // (n_row // d)
    x4 = cur.reshape(n_row // (2 * d), 2, m, cur.shape[1])
    bit = (r // d) % 2
    keep = lax.dynamic_index_in_dim(x4, bit, axis=1, keepdims=False)
    send = lax.dynamic_index_in_dim(x4, 1 - bit, axis=1, keepdims=False)
    got = lax.ppermute(send.astype(jnp.bfloat16), "row", [(i, i ^ d) for i in range(n_row)])
    return (keep.astype(jnp.float32) + got.astype(jnp.float32)).reshape(-1, cur.shape[1])


def make_on_device(n_row, n_col, order):
    ring = Ring(order)
    levels = []
    d = 1
    while d < n_row:
        levels.append(d)
        d *= 2

    def on_device(tokens, gate_weight, up_weight):
        local = tokens.shape[0]
        shares = share_sizes(local)
        offs = [sum(shares[:i]) for i in range(len(shares))]
        group = n_col // n_row
        units = gate_weight.shape[1]
        us = units // SPLIT_UNITS
        per_share = 2 * SPLIT_UNITS

        st = ring.init(tokens[:shares[0]])
        for s in range(1, ring.steps + 1):
            st = ring.step(st, s)
        piece = ring.result(st)

        tiles = []
        for h in range(len(shares)):
            for w in range(2):
                for j in range(SPLIT_UNITS):
                    tiles.append((h, w, j))

        jobs = []
        done = {}
        nxt = None
        t = 0
        while t < len(tiles) or jobs:
            carry = {}
            for job in jobs:
                job[2] = reduce_level(job[2], levels[job[1]], n_row)
                job[1] += 1
            if t < len(tiles):
                h, w, j = tiles[t]
                if t % per_share == 0 and h + 1 < len(shares):
                    nxt = {"st": ring.init(tokens[offs[h + 1]:offs[h + 1] + shares[h + 1]]), "s": 1}
                if nxt is not None and nxt["s"] <= ring.steps:
                    nxt["st"] = ring.step(nxt["st"], nxt["s"])
                    nxt["s"] += 1
                weight = gate_weight if w == 0 else up_weight
                out = jnp.dot(
                    piece, weight[:, j * us:(j + 1) * us], preferred_element_type=jnp.float32
                ).astype(jnp.bfloat16)
                new_job = [t, 0, out]
            else:
                new_job = None
            finished = [jb for jb in jobs if jb[1] == len(levels)]
            jobs = [jb for jb in jobs if jb[1] < len(levels)]
            for jb in finished:
                done[jb[0]] = jb[2]
            if new_job is not None:
                if levels:
                    jobs.append(new_job)
                else:
                    done[new_job[0]] = new_job[2].astype(jnp.float32)
            carry["piece"] = piece
            carry["jobs"] = [jb[2] for jb in jobs]
            carry["nxt"] = nxt["st"] if nxt is not None else None
            carry["done"] = done
            carry = lax.optimization_barrier(carry)
            piece = carry["piece"]
            for jb, a in zip(jobs, carry["jobs"]):
                jb[2] = a
            if nxt is not None:
                nxt["st"] = carry["nxt"]
            done = carry["done"]
            t += 1
            if t < len(tiles) and t % per_share == 0 and nxt is not None:
                while nxt["s"] <= ring.steps:
                    nxt["st"] = ring.step(nxt["st"], nxt["s"])
                    nxt["s"] += 1
                piece = ring.result(nxt["st"])
                nxt = None

        def assemble(w):
            parts = []
            for h in range(len(shares)):
                base = (h * 2 + w) * SPLIT_UNITS
                x = jnp.concatenate([done[base + j] for j in range(SPLIT_UNITS)], axis=1)
                parts.append(x.reshape(group, shares[h], units))
            return jnp.concatenate(parts, axis=1).reshape(group * local, units)

        gate = assemble(0)
        up = assemble(1)
        return (jax.nn.silu(gate) * up).astype(jnp.bfloat16)

    return on_device


def solution(mesh):
    placed = (P("col", "row"), P("row", "col"), P("row", "col"))
    fn = make_on_device(mesh.shape["row"], mesh.shape["col"], ring_order(mesh))
    return jax.shard_map(
        fn, mesh=mesh, in_specs=placed, out_specs=P("row", "col"), check_vma=False
    )
```

```python
import jax
import jax.numpy as jnp
import numpy as np
from jax import lax
from jax.sharding import PartitionSpec as P

HALVES = 2
SPLIT_UNITS = 2


def ring_order(mesh):
    col = mesh.devices[0]
    n = len(col)
    try:
        zs = sorted({d.coords[2] for d in col})
        xs = sorted({d.coords[0] for d in col})
        at = {(zs.index(d.coords[2]), xs.index(d.coords[0])): i for i, d in enumerate(col)}
    except Exception:
        return list(range(n))
    a, b = len(zs), len(xs)
    if a * b != n or len(at) != n or a % 2 or b < 2:
        return list(range(n))
    cells = [(z, 0) for z in range(a)]
    for k, z in enumerate(range(a - 1, -1, -1)):
        span = range(1, b) if k % 2 == 0 else range(b - 1, 0, -1)
        cells += [(z, x) for x in span]
    return [at[c] for c in cells]


class Ring:
    def __init__(self, order):
        self.order = order
        n = len(order)
        self.n = n
        pos = np.zeros(n, np.int32)
        for q, c in enumerate(order):
            pos[c] = q
        self.pos = pos
        self.fwd_pairs = [(order[q], order[(q + 1) % n]) for q in range(n)]
        self.bwd_pairs = [(order[q], order[(q - 1) % n]) for q in range(n)]
        self.steps = n // 2
        self.back_steps = n - 1 - n // 2

    def init(self, x):
        n = self.n
        c = lax.axis_index("col")
        buf = jnp.zeros((n,) + x.shape, x.dtype)
        buf = lax.dynamic_update_slice(buf, x[None], (c, 0, 0))
        return {"buf": buf, "f": x, "b": x}

    def step(self, st, s):
        n = self.n
        c = lax.axis_index("col")
        p = jnp.asarray(self.pos)[c]
        order_t = jnp.asarray(np.array(self.order, np.int32))
        buf = st["buf"]
        f = lax.ppermute(st["f"], "col", self.fwd_pairs)
        buf = lax.dynamic_update_slice(buf, f[None], (order_t[(p - s) % n], 0, 0))
        b = st["b"]
        if s <= self.back_steps:
            b = lax.ppermute(b, "col", self.bwd_pairs)
            buf = lax.dynamic_update_slice(buf, b[None], (order_t[(p + s) % n], 0, 0))
        return {"buf": buf, "f": f, "b": b}

    def result(self, st):
        buf = st["buf"]
        return buf.reshape((-1,) + buf.shape[2:])


def reduce_level(cur, d, n_row):
    r = lax.axis_index("row")
    m = cur.shape[0] // (n_row // d)
    x4 = cur.reshape(n_row // (2 * d), 2, m, cur.shape[1])
    bit = (r // d) % 2
    keep = lax.dynamic_index_in_dim(x4, bit, axis=1, keepdims=False)
    send = lax.dynamic_index_in_dim(x4, 1 - bit, axis=1, keepdims=False)
    got = lax.ppermute(send.astype(jnp.bfloat16), "row", [(i, i ^ d) for i in range(n_row)])
    return (keep.astype(jnp.float32) + got.astype(jnp.float32)).reshape(-1, cur.shape[1])


def reduce_direct(cur, n_row):
    r = lax.axis_index("row")
    x = cur.reshape(n_row, cur.shape[0] // n_row, cur.shape[1])
    total = lax.dynamic_index_in_dim(x, r, axis=0, keepdims=False).astype(jnp.float32)
    for d in range(1, n_row):
        send = lax.dynamic_index_in_dim(x, r ^ d, axis=0, keepdims=False)
        got = lax.ppermute(send.astype(jnp.bfloat16), "row", [(i, i ^ d) for i in range(n_row)])
        total = total + got.astype(jnp.float32)
    return total


def make_on_device(n_row, n_col, order):
    ring = Ring(order)
    levels = []
    d = 1
    while d < n_row:
        levels.append(d)
        d *= 2

    def on_device(tokens, gate_weight, up_weight):
        local = tokens.shape[0]
        tc = local // HALVES
        group = n_col // n_row
        units = gate_weight.shape[1]
        us = units // SPLIT_UNITS

        st = ring.init(tokens[:tc])
        for s in range(1, ring.steps + 1):
            st = ring.step(st, s)
        piece = ring.result(st)
        piece, tokens = lax.optimization_barrier((piece, tokens))

        tiles = []
        for h in range(HALVES):
            for w in range(2):
                for j in range(SPLIT_UNITS):
                    tiles.append((h, w, j))

        jobs = []
        done = {}
        nxt = None
        t = 0
        while t < len(tiles) or jobs:
            carry = {}
            for job in jobs:
                if job[0] == len(tiles) - 1:
                    job[2] = reduce_direct(job[2], n_row)
                    job[1] = len(levels)
                else:
                    job[2] = reduce_level(job[2], levels[job[1]], n_row)
                    job[1] += 1
            if t < len(tiles):
                h, w, j = tiles[t]
                first_of_share = t % (2 * SPLIT_UNITS) == 0
                if first_of_share and h + 1 < HALVES:
                    nxt = {"st": ring.init(tokens[(h + 1) * tc:(h + 2) * tc]), "s": 1}
                if nxt is not None and nxt["s"] <= ring.steps:
                    nxt["st"] = ring.step(nxt["st"], nxt["s"])
                    nxt["s"] += 1
                weight = gate_weight if w == 0 else up_weight
                out = jnp.dot(
                    piece, weight[:, j * us:(j + 1) * us], preferred_element_type=jnp.float32
                ).astype(jnp.bfloat16)
                new_job = [t, 0, out]
            else:
                new_job = None
            finished = [jb for jb in jobs if jb[1] == len(levels)]
            jobs = [jb for jb in jobs if jb[1] < len(levels)]
            for jb in finished:
                done[jb[0]] = jb[2]
            if new_job is not None:
                if levels:
                    jobs.append(new_job)
                else:
                    done[new_job[0]] = new_job[2].astype(jnp.float32)
            carry["piece"] = piece
            carry["jobs"] = [jb[2] for jb in jobs]
            carry["nxt"] = nxt["st"] if nxt is not None else None
            carry["done"] = done
            carry = lax.optimization_barrier(carry)
            piece = carry["piece"]
            for jb, a in zip(jobs, carry["jobs"]):
                jb[2] = a
            if nxt is not None:
                nxt["st"] = carry["nxt"]
            done = carry["done"]
            t += 1
            if t < len(tiles) and t % (2 * SPLIT_UNITS) == 0 and nxt is not None:
                while nxt["s"] <= ring.steps:
                    nxt["st"] = ring.step(nxt["st"], nxt["s"])
                    nxt["s"] += 1
                piece = ring.result(nxt["st"])
                nxt = None

        def assemble(w):
            parts = []
            for h in range(HALVES):
                base = (h * 2 + w) * SPLIT_UNITS
                parts.append(jnp.concatenate([done[base + j] for j in range(SPLIT_UNITS)], axis=1))
            x = jnp.stack(parts).reshape(HALVES, group, tc, units)
            return x.transpose(1, 0, 2, 3).reshape(group * HALVES * tc, units)

        gate = assemble(0)
        up = assemble(1)
        return (jax.nn.silu(gate) * up).astype(jnp.bfloat16)

    return on_device


def solution(mesh):
    placed = (P("col", "row"), P("row", "col"), P("row", "col"))
    fn = make_on_device(mesh.shape["row"], mesh.shape["col"], ring_order(mesh))
    return jax.shard_map(
        fn, mesh=mesh, in_specs=placed, out_specs=P("row", "col"), check_vma=False
    )
```

```python
import jax
import jax.numpy as jnp
import numpy as np
from jax import lax
from jax.sharding import PartitionSpec as P

HALVES = 2


def tile_widths(units, last):
    half = units // 2
    if not last:
        return [half, units - half]
    rest = units - half
    small = max(128, (rest // 3) // 128 * 128)
    return [half, rest - small, small]


def ring_order(mesh):
    col = mesh.devices[0]
    n = len(col)
    try:
        zs = sorted({d.coords[2] for d in col})
        xs = sorted({d.coords[0] for d in col})
        at = {(zs.index(d.coords[2]), xs.index(d.coords[0])): i for i, d in enumerate(col)}
    except Exception:
        return list(range(n))
    a, b = len(zs), len(xs)
    if a * b != n or len(at) != n or a % 2 or b < 2:
        return list(range(n))
    cells = [(z, 0) for z in range(a)]
    for k, z in enumerate(range(a - 1, -1, -1)):
        span = range(1, b) if k % 2 == 0 else range(b - 1, 0, -1)
        cells += [(z, x) for x in span]
    return [at[c] for c in cells]


class Ring:
    def __init__(self, order):
        self.order = order
        n = len(order)
        self.n = n
        pos = np.zeros(n, np.int32)
        for q, c in enumerate(order):
            pos[c] = q
        self.pos = pos
        self.fwd_pairs = [(order[q], order[(q + 1) % n]) for q in range(n)]
        self.bwd_pairs = [(order[q], order[(q - 1) % n]) for q in range(n)]
        self.steps = n // 2
        self.back_steps = n - 1 - n // 2

    def init(self, x):
        n = self.n
        c = lax.axis_index("col")
        buf = jnp.zeros((n,) + x.shape, x.dtype)
        buf = lax.dynamic_update_slice(buf, x[None], (c, 0, 0))
        return {"buf": buf, "f": x, "b": x}

    def step(self, st, s):
        n = self.n
        c = lax.axis_index("col")
        p = jnp.asarray(self.pos)[c]
        order_t = jnp.asarray(np.array(self.order, np.int32))
        buf = st["buf"]
        f = lax.ppermute(st["f"], "col", self.fwd_pairs)
        buf = lax.dynamic_update_slice(buf, f[None], (order_t[(p - s) % n], 0, 0))
        b = st["b"]
        if s <= self.back_steps:
            b = lax.ppermute(b, "col", self.bwd_pairs)
            buf = lax.dynamic_update_slice(buf, b[None], (order_t[(p + s) % n], 0, 0))
        return {"buf": buf, "f": f, "b": b}

    def result(self, st):
        buf = st["buf"]
        return buf.reshape((-1,) + buf.shape[2:])


def reduce_level(cur, d, n_row):
    r = lax.axis_index("row")
    m = cur.shape[0] // (n_row // d)
    x4 = cur.reshape(n_row // (2 * d), 2, m, cur.shape[1])
    bit = (r // d) % 2
    keep = lax.dynamic_index_in_dim(x4, bit, axis=1, keepdims=False)
    send = lax.dynamic_index_in_dim(x4, 1 - bit, axis=1, keepdims=False)
    got = lax.ppermute(send.astype(jnp.bfloat16), "row", [(i, i ^ d) for i in range(n_row)])
    return (keep.astype(jnp.float32) + got.astype(jnp.float32)).reshape(-1, cur.shape[1])


def make_on_device(n_row, n_col, order):
    ring = Ring(order)
    levels = []
    d = 1
    while d < n_row:
        levels.append(d)
        d *= 2

    def on_device(tokens, gate_weight, up_weight):
        local = tokens.shape[0]
        tc = local // HALVES
        group = n_col // n_row
        units = gate_weight.shape[1]

        st = ring.init(tokens[:tc])
        for s in range(1, ring.steps + 1):
            st = ring.step(st, s)
        piece = ring.result(st)
        piece, tokens = lax.optimization_barrier((piece, tokens))

        tiles = []
        for h in range(HALVES):
            for w in range(2):
                start = 0
                for width in tile_widths(units, h == HALVES - 1 and w == 1):
                    tiles.append((h, w, start, width))
                    start += width
        firsts = [i for i, tl in enumerate(tiles) if i == 0 or tl[0] != tiles[i - 1][0]]

        jobs = []
        done = {}
        nxt = None
        t = 0
        while t < len(tiles) or jobs:
            carry = {}
            for job in jobs:
                job[2] = reduce_level(job[2], levels[job[1]], n_row)
                job[1] += 1
            if t < len(tiles):
                h, w, start, width = tiles[t]
                if t in firsts and h + 1 < HALVES:
                    nxt = {"st": ring.init(tokens[(h + 1) * tc:(h + 2) * tc]), "s": 1}
                if nxt is not None and nxt["s"] <= ring.steps:
                    nxt["st"] = ring.step(nxt["st"], nxt["s"])
                    nxt["s"] += 1
                weight = gate_weight if w == 0 else up_weight
                out = jnp.dot(
                    piece, weight[:, start:start + width], preferred_element_type=jnp.float32
                ).astype(jnp.bfloat16)
                new_job = [t, 0, out]
            else:
                new_job = None
            finished = [jb for jb in jobs if jb[1] == len(levels)]
            jobs = [jb for jb in jobs if jb[1] < len(levels)]
            for jb in finished:
                done[jb[0]] = jb[2]
            if new_job is not None:
                if levels:
                    jobs.append(new_job)
                else:
                    done[new_job[0]] = new_job[2].astype(jnp.float32)
            carry["piece"] = piece
            carry["jobs"] = [jb[2] for jb in jobs]
            carry["nxt"] = nxt["st"] if nxt is not None else None
            carry["done"] = done
            carry = lax.optimization_barrier(carry)
            piece = carry["piece"]
            for jb, a in zip(jobs, carry["jobs"]):
                jb[2] = a
            if nxt is not None:
                nxt["st"] = carry["nxt"]
            done = carry["done"]
            t += 1
            if t < len(tiles) and t in firsts and nxt is not None:
                while nxt["s"] <= ring.steps:
                    nxt["st"] = ring.step(nxt["st"], nxt["s"])
                    nxt["s"] += 1
                piece = ring.result(nxt["st"])
                nxt = None

        def assemble(w):
            parts = []
            for h in range(HALVES):
                ids = [i for i, tl in enumerate(tiles) if tl[0] == h and tl[1] == w]
                parts.append(jnp.concatenate([done[i] for i in ids], axis=1))
            x = jnp.stack(parts).reshape(HALVES, group, tc, units)
            return x.transpose(1, 0, 2, 3).reshape(group * HALVES * tc, units)

        gate = assemble(0)
        up = assemble(1)
        return (jax.nn.silu(gate) * up).astype(jnp.bfloat16)

    return on_device


def solution(mesh):
    placed = (P("col", "row"), P("row", "col"), P("row", "col"))
    fn = make_on_device(mesh.shape["row"], mesh.shape["col"], ring_order(mesh))
    return jax.shard_map(
        fn, mesh=mesh, in_specs=placed, out_specs=P("row", "col"), check_vma=False
    )
```

```python
import jax
import jax.numpy as jnp
import numpy as np
from jax import lax
from jax.sharding import PartitionSpec as P

HALVES = 2


def tile_widths(units, last):
    half = units // 2
    if not last:
        return [half, units - half]
    rest = units - half
    small = max(128, (rest // 3) // 128 * 128)
    return [half, rest - small, small]


def ring_order(mesh):
    col = mesh.devices[0]
    n = len(col)
    try:
        zs = sorted({d.coords[2] for d in col})
        xs = sorted({d.coords[0] for d in col})
        at = {(zs.index(d.coords[2]), xs.index(d.coords[0])): i for i, d in enumerate(col)}
    except Exception:
        return list(range(n))
    a, b = len(zs), len(xs)
    if a * b != n or len(at) != n or a % 2 or b < 2:
        return list(range(n))
    cells = [(z, 0) for z in range(a)]
    for k, z in enumerate(range(a - 1, -1, -1)):
        span = range(1, b) if k % 2 == 0 else range(b - 1, 0, -1)
        cells += [(z, x) for x in span]
    return [at[c] for c in cells]


class Ring:
    def __init__(self, order):
        self.order = order
        n = len(order)
        self.n = n
        pos = np.zeros(n, np.int32)
        for q, c in enumerate(order):
            pos[c] = q
        self.pos = pos
        self.fwd_pairs = [(order[q], order[(q + 1) % n]) for q in range(n)]
        self.bwd_pairs = [(order[q], order[(q - 1) % n]) for q in range(n)]
        self.steps = n // 2
        self.back_steps = n - 1 - n // 2

    def init(self, x):
        n = self.n
        c = lax.axis_index("col")
        buf = jnp.zeros((n,) + x.shape, x.dtype)
        buf = lax.dynamic_update_slice(buf, x[None], (c, 0, 0))
        return {"buf": buf, "f": x, "b": x}

    def step(self, st, s):
        n = self.n
        c = lax.axis_index("col")
        p = jnp.asarray(self.pos)[c]
        order_t = jnp.asarray(np.array(self.order, np.int32))
        buf = st["buf"]
        b = st["b"]
        if s == self.steps and self.back_steps < s and n > 2:
            k2 = b.shape[1] // 2
            f = lax.ppermute(st["f"][:, :k2], "col", self.fwd_pairs)
            b = lax.ppermute(b[:, k2:], "col", self.bwd_pairs)
            src = order_t[(p - s) % n]
            buf = lax.dynamic_update_slice(buf, f[None], (src, 0, 0))
            buf = lax.dynamic_update_slice(buf, b[None], (src, 0, k2))
            return {"buf": buf, "f": f, "b": b}
        f = lax.ppermute(st["f"], "col", self.fwd_pairs)
        buf = lax.dynamic_update_slice(buf, f[None], (order_t[(p - s) % n], 0, 0))
        if s <= self.back_steps:
            b = lax.ppermute(b, "col", self.bwd_pairs)
            buf = lax.dynamic_update_slice(buf, b[None], (order_t[(p + s) % n], 0, 0))
        return {"buf": buf, "f": f, "b": b}

    def result(self, st):
        buf = st["buf"]
        return buf.reshape((-1,) + buf.shape[2:])


def reduce_level(cur, d, n_row):
    r = lax.axis_index("row")
    m = cur.shape[0] // (n_row // d)
    x4 = cur.reshape(n_row // (2 * d), 2, m, cur.shape[1])
    bit = (r // d) % 2
    keep = lax.dynamic_index_in_dim(x4, bit, axis=1, keepdims=False)
    send = lax.dynamic_index_in_dim(x4, 1 - bit, axis=1, keepdims=False)
    got = lax.ppermute(send.astype(jnp.bfloat16), "row", [(i, i ^ d) for i in range(n_row)])
    return (keep.astype(jnp.float32) + got.astype(jnp.float32)).reshape(-1, cur.shape[1])


def make_on_device(n_row, n_col, order):
    ring = Ring(order)
    levels = []
    d = 1
    while d < n_row:
        levels.append(d)
        d *= 2

    def on_device(tokens, gate_weight, up_weight):
        local = tokens.shape[0]
        tc = local // HALVES
        group = n_col // n_row
        units = gate_weight.shape[1]

        st = ring.init(tokens[:tc])
        for s in range(1, ring.steps + 1):
            st = ring.step(st, s)
        piece = ring.result(st)
        piece, tokens = lax.optimization_barrier((piece, tokens))

        tiles = []
        for h in range(HALVES):
            for w in range(2):
                start = 0
                for width in tile_widths(units, h == HALVES - 1 and w == 1):
                    tiles.append((h, w, start, width))
                    start += width
        firsts = [i for i, tl in enumerate(tiles) if i == 0 or tl[0] != tiles[i - 1][0]]

        jobs = []
        done = {}
        nxt = None
        t = 0
        while t < len(tiles) or jobs:
            carry = {}
            for job in jobs:
                job[2] = reduce_level(job[2], levels[job[1]], n_row)
                job[1] += 1
            if t < len(tiles):
                h, w, start, width = tiles[t]
                if t in firsts and h + 1 < HALVES:
                    nxt = {"st": ring.init(tokens[(h + 1) * tc:(h + 2) * tc]), "s": 1}
                if nxt is not None and nxt["s"] <= ring.steps:
                    nxt["st"] = ring.step(nxt["st"], nxt["s"])
                    nxt["s"] += 1
                weight = gate_weight if w == 0 else up_weight
                out = jnp.dot(
                    piece, weight[:, start:start + width], preferred_element_type=jnp.float32
                ).astype(jnp.bfloat16)
                new_job = [t, 0, out]
            else:
                new_job = None
            finished = [jb for jb in jobs if jb[1] == len(levels)]
            jobs = [jb for jb in jobs if jb[1] < len(levels)]
            for jb in finished:
                done[jb[0]] = jb[2]
            if new_job is not None:
                if levels:
                    jobs.append(new_job)
                else:
                    done[new_job[0]] = new_job[2].astype(jnp.float32)
            carry["piece"] = piece
            carry["jobs"] = [jb[2] for jb in jobs]
            carry["nxt"] = nxt["st"] if nxt is not None else None
            carry["done"] = done
            carry = lax.optimization_barrier(carry)
            piece = carry["piece"]
            for jb, a in zip(jobs, carry["jobs"]):
                jb[2] = a
            if nxt is not None:
                nxt["st"] = carry["nxt"]
            done = carry["done"]
            t += 1
            if t < len(tiles) and t in firsts and nxt is not None:
                while nxt["s"] <= ring.steps:
                    nxt["st"] = ring.step(nxt["st"], nxt["s"])
                    nxt["s"] += 1
                piece = ring.result(nxt["st"])
                nxt = None

        def assemble(w):
            parts = []
            for h in range(HALVES):
                ids = [i for i, tl in enumerate(tiles) if tl[0] == h and tl[1] == w]
                parts.append(jnp.concatenate([done[i] for i in ids], axis=1))
            x = jnp.stack(parts).reshape(HALVES, group, tc, units)
            return x.transpose(1, 0, 2, 3).reshape(group * HALVES * tc, units)

        gate = assemble(0)
        up = assemble(1)
        return (jax.nn.silu(gate) * up).astype(jnp.bfloat16)

    return on_device


def solution(mesh):
    placed = (P("col", "row"), P("row", "col"), P("row", "col"))
    fn = make_on_device(mesh.shape["row"], mesh.shape["col"], ring_order(mesh))
    return jax.shard_map(
        fn, mesh=mesh, in_specs=placed, out_specs=P("row", "col"), check_vma=False
    )
```

```python
import jax
import jax.numpy as jnp
import numpy as np
from jax import lax
from jax.sharding import PartitionSpec as P

HALVES = 2


def tile_widths(units, last):
    half = units // 2
    if not last:
        return [half, units - half]
    taper = [9 * 128, 5 * 128, 2 * 128]
    if units - sum(taper) >= taper[0]:
        return [units - sum(taper)] + taper
    rest = units - half
    small = max(128, (rest // 3) // 128 * 128)
    return [half, rest - small, small]


def ring_order(mesh):
    col = mesh.devices[0]
    n = len(col)
    try:
        zs = sorted({d.coords[2] for d in col})
        xs = sorted({d.coords[0] for d in col})
        at = {(zs.index(d.coords[2]), xs.index(d.coords[0])): i for i, d in enumerate(col)}
    except Exception:
        return list(range(n))
    a, b = len(zs), len(xs)
    if a * b != n or len(at) != n or a % 2 or b < 2:
        return list(range(n))
    cells = [(z, 0) for z in range(a)]
    for k, z in enumerate(range(a - 1, -1, -1)):
        span = range(1, b) if k % 2 == 0 else range(b - 1, 0, -1)
        cells += [(z, x) for x in span]
    return [at[c] for c in cells]


class Ring:
    def __init__(self, order):
        self.order = order
        n = len(order)
        self.n = n
        pos = np.zeros(n, np.int32)
        for q, c in enumerate(order):
            pos[c] = q
        self.pos = pos
        self.fwd_pairs = [(order[q], order[(q + 1) % n]) for q in range(n)]
        self.bwd_pairs = [(order[q], order[(q - 1) % n]) for q in range(n)]
        self.steps = n // 2
        self.back_steps = n - 1 - n // 2

    def init(self, x):
        n = self.n
        c = lax.axis_index("col")
        buf = jnp.zeros((n,) + x.shape, x.dtype)
        buf = lax.dynamic_update_slice(buf, x[None], (c, 0, 0))
        return {"buf": buf, "f": x, "b": x}

    def step(self, st, s):
        n = self.n
        c = lax.axis_index("col")
        p = jnp.asarray(self.pos)[c]
        order_t = jnp.asarray(np.array(self.order, np.int32))
        buf = st["buf"]
        b = st["b"]
        if s == self.steps and self.back_steps < s and n > 2:
            k2 = b.shape[1] // 2
            f = lax.ppermute(st["f"][:, :k2], "col", self.fwd_pairs)
            b = lax.ppermute(b[:, k2:], "col", self.bwd_pairs)
            src = order_t[(p - s) % n]
            buf = lax.dynamic_update_slice(buf, f[None], (src, 0, 0))
            buf = lax.dynamic_update_slice(buf, b[None], (src, 0, k2))
            return {"buf": buf, "f": f, "b": b}
        f = lax.ppermute(st["f"], "col", self.fwd_pairs)
        buf = lax.dynamic_update_slice(buf, f[None], (order_t[(p - s) % n], 0, 0))
        if s <= self.back_steps:
            b = lax.ppermute(b, "col", self.bwd_pairs)
            buf = lax.dynamic_update_slice(buf, b[None], (order_t[(p + s) % n], 0, 0))
        return {"buf": buf, "f": f, "b": b}

    def result(self, st):
        buf = st["buf"]
        return buf.reshape((-1,) + buf.shape[2:])


def reduce_level(cur, d, n_row):
    r = lax.axis_index("row")
    m = cur.shape[0] // (n_row // d)
    x4 = cur.reshape(n_row // (2 * d), 2, m, cur.shape[1])
    bit = (r // d) % 2
    keep = lax.dynamic_index_in_dim(x4, bit, axis=1, keepdims=False)
    send = lax.dynamic_index_in_dim(x4, 1 - bit, axis=1, keepdims=False)
    got = lax.ppermute(send.astype(jnp.bfloat16), "row", [(i, i ^ d) for i in range(n_row)])
    return (keep.astype(jnp.float32) + got.astype(jnp.float32)).reshape(-1, cur.shape[1])


def make_on_device(n_row, n_col, order):
    ring = Ring(order)
    levels = []
    d = 1
    while d < n_row:
        levels.append(d)
        d *= 2

    def on_device(tokens, gate_weight, up_weight):
        local = tokens.shape[0]
        tc = local // HALVES
        group = n_col // n_row
        units = gate_weight.shape[1]

        st = ring.init(tokens[:tc])
        for s in range(1, ring.steps + 1):
            st = ring.step(st, s)
        piece = ring.result(st)
        piece, tokens = lax.optimization_barrier((piece, tokens))

        tiles = []
        for h in range(HALVES):
            for w in range(2):
                start = 0
                for width in tile_widths(units, h == HALVES - 1 and w == 1):
                    tiles.append((h, w, start, width))
                    start += width
        firsts = [i for i, tl in enumerate(tiles) if i == 0 or tl[0] != tiles[i - 1][0]]

        jobs = []
        done = {}
        nxt = None
        t = 0
        while t < len(tiles) or jobs:
            carry = {}
            for job in jobs:
                job[2] = reduce_level(job[2], levels[job[1]], n_row)
                job[1] += 1
            if t < len(tiles):
                h, w, start, width = tiles[t]
                if t in firsts and h + 1 < HALVES:
                    nxt = {"st": ring.init(tokens[(h + 1) * tc:(h + 2) * tc]), "s": 1}
                if nxt is not None and nxt["s"] <= ring.steps:
                    nxt["st"] = ring.step(nxt["st"], nxt["s"])
                    nxt["s"] += 1
                weight = gate_weight if w == 0 else up_weight
                out = jnp.dot(
                    piece, weight[:, start:start + width], preferred_element_type=jnp.float32
                ).astype(jnp.bfloat16)
                new_job = [t, 0, out]
            else:
                new_job = None
            finished = [jb for jb in jobs if jb[1] == len(levels)]
            jobs = [jb for jb in jobs if jb[1] < len(levels)]
            for jb in finished:
                done[jb[0]] = jb[2]
            if new_job is not None:
                if levels:
                    jobs.append(new_job)
                else:
                    done[new_job[0]] = new_job[2].astype(jnp.float32)
            carry["piece"] = piece
            carry["jobs"] = [jb[2] for jb in jobs]
            carry["nxt"] = nxt["st"] if nxt is not None else None
            carry["done"] = done
            carry = lax.optimization_barrier(carry)
            piece = carry["piece"]
            for jb, a in zip(jobs, carry["jobs"]):
                jb[2] = a
            if nxt is not None:
                nxt["st"] = carry["nxt"]
            done = carry["done"]
            t += 1
            if t < len(tiles) and t in firsts and nxt is not None:
                while nxt["s"] <= ring.steps:
                    nxt["st"] = ring.step(nxt["st"], nxt["s"])
                    nxt["s"] += 1
                piece = ring.result(nxt["st"])
                nxt = None

        def assemble(w):
            parts = []
            for h in range(HALVES):
                ids = [i for i, tl in enumerate(tiles) if tl[0] == h and tl[1] == w]
                parts.append(jnp.concatenate([done[i] for i in ids], axis=1))
            x = jnp.stack(parts).reshape(HALVES, group, tc, units)
            return x.transpose(1, 0, 2, 3).reshape(group * HALVES * tc, units)

        gate = assemble(0)
        up = assemble(1)
        return (jax.nn.silu(gate) * up).astype(jnp.bfloat16)

    return on_device


def solution(mesh):
    placed = (P("col", "row"), P("row", "col"), P("row", "col"))
    fn = make_on_device(mesh.shape["row"], mesh.shape["col"], ring_order(mesh))
    return jax.shard_map(
        fn, mesh=mesh, in_specs=placed, out_specs=P("row", "col"), check_vma=False
    )
```

```python
import jax
import jax.numpy as jnp
import numpy as np
from jax import lax
from jax.sharding import PartitionSpec as P

HALVES = 2


def tile_widths(units, last):
    half = units // 2
    if not last:
        return [half, units - half]
    rest = units - half
    small = max(128, (rest // 3) // 128 * 128)
    return [half, rest - small, small]


def ring_order(mesh):
    col = mesh.devices[0]
    n = len(col)
    try:
        zs = sorted({d.coords[2] for d in col})
        xs = sorted({d.coords[0] for d in col})
        at = {(zs.index(d.coords[2]), xs.index(d.coords[0])): i for i, d in enumerate(col)}
    except Exception:
        return list(range(n))
    a, b = len(zs), len(xs)
    if a * b != n or len(at) != n or a % 2 or b < 2:
        return list(range(n))
    cells = [(z, 0) for z in range(a)]
    for k, z in enumerate(range(a - 1, -1, -1)):
        span = range(1, b) if k % 2 == 0 else range(b - 1, 0, -1)
        cells += [(z, x) for x in span]
    return [at[c] for c in cells]


class Ring:
    def __init__(self, order):
        self.order = order
        n = len(order)
        self.n = n
        pos = np.zeros(n, np.int32)
        for q, c in enumerate(order):
            pos[c] = q
        self.pos = pos
        self.fwd_pairs = [(order[q], order[(q + 1) % n]) for q in range(n)]
        self.bwd_pairs = [(order[q], order[(q - 1) % n]) for q in range(n)]
        self.steps = n // 2
        self.back_steps = n - 1 - n // 2

    def init(self, x):
        n = self.n
        c = lax.axis_index("col")
        buf = jnp.zeros((n,) + x.shape, x.dtype)
        buf = lax.dynamic_update_slice(buf, x[None], (c, 0, 0))
        return {"buf": buf, "f": x, "b": x}

    def step(self, st, s):
        n = self.n
        c = lax.axis_index("col")
        p = jnp.asarray(self.pos)[c]
        order_t = jnp.asarray(np.array(self.order, np.int32))
        buf = st["buf"]
        b = st["b"]
        if s == self.steps and self.back_steps < s and n > 2:
            k2 = b.shape[1] // 2
            f = lax.ppermute(st["f"][:, :k2], "col", self.fwd_pairs)
            b = lax.ppermute(b[:, k2:], "col", self.bwd_pairs)
            src = order_t[(p - s) % n]
            buf = lax.dynamic_update_slice(buf, f[None], (src, 0, 0))
            buf = lax.dynamic_update_slice(buf, b[None], (src, 0, k2))
            return {"buf": buf, "f": f, "b": b}
        f = lax.ppermute(st["f"], "col", self.fwd_pairs)
        buf = lax.dynamic_update_slice(buf, f[None], (order_t[(p - s) % n], 0, 0))
        if s <= self.back_steps:
            b = lax.ppermute(b, "col", self.bwd_pairs)
            buf = lax.dynamic_update_slice(buf, b[None], (order_t[(p + s) % n], 0, 0))
        return {"buf": buf, "f": f, "b": b}

    def result(self, st):
        buf = st["buf"]
        return buf.reshape((-1,) + buf.shape[2:])


def reduce_level(cur, d, n_row):
    r = lax.axis_index("row")
    m = cur.shape[0] // (n_row // d)
    x4 = cur.reshape(n_row // (2 * d), 2, m, cur.shape[1])
    bit = (r // d) % 2
    keep = lax.dynamic_index_in_dim(x4, bit, axis=1, keepdims=False)
    send = lax.dynamic_index_in_dim(x4, 1 - bit, axis=1, keepdims=False)
    got = lax.ppermute(send.astype(jnp.bfloat16), "row", [(i, i ^ d) for i in range(n_row)])
    return (keep.astype(jnp.float32) + got.astype(jnp.float32)).reshape(-1, cur.shape[1])


def make_on_device(n_row, n_col, order):
    ring = Ring(order)
    levels = []
    d = 1
    while d < n_row:
        levels.append(d)
        d *= 2

    def on_device(tokens, gate_weight, up_weight):
        local = tokens.shape[0]
        tc = local // HALVES
        group = n_col // n_row
        units = gate_weight.shape[1]

        st = ring.init(tokens[:tc])
        for s in range(1, ring.steps + 1):
            st = ring.step(st, s)
        piece = ring.result(st)
        piece, tokens = lax.optimization_barrier((piece, tokens))

        tiles = []
        for h in range(HALVES):
            for w in range(2):
                start = 0
                for width in tile_widths(units, h == HALVES - 1 and w == 1):
                    tiles.append((h, w, start, width))
                    start += width
        firsts = [i for i, tl in enumerate(tiles) if i == 0 or tl[0] != tiles[i - 1][0]]

        jobs = []
        done = {}
        nxt = None
        t = 0
        while t < len(tiles) or jobs:
            carry = {}
            for job in jobs:
                job[2] = reduce_level(job[2], levels[job[1]], n_row)
                job[1] += 1
            if t < len(tiles):
                h, w, start, width = tiles[t]
                if t in firsts and h + 1 < HALVES:
                    nxt = {"st": ring.init(tokens[(h + 1) * tc:(h + 2) * tc]), "s": 1}
                if nxt is not None and nxt["s"] <= ring.steps:
                    nxt["st"] = ring.step(nxt["st"], nxt["s"])
                    nxt["s"] += 1
                weight = gate_weight if w == 0 else up_weight
                out = jnp.dot(
                    piece, weight[:, start:start + width], preferred_element_type=jnp.float32
                ).astype(jnp.bfloat16)
                new_job = [t, 0, out]
            else:
                new_job = None
            finished = [jb for jb in jobs if jb[1] == len(levels)]
            jobs = [jb for jb in jobs if jb[1] < len(levels)]
            for jb in finished:
                done[jb[0]] = jb[2]
            if new_job is not None:
                if levels:
                    jobs.append(new_job)
                else:
                    done[new_job[0]] = new_job[2].astype(jnp.float32)
            carry["piece"] = piece
            carry["jobs"] = [jb[2] for jb in jobs]
            carry["nxt"] = nxt["st"] if nxt is not None else None
            carry["done"] = done
            if t + 1 < len(tiles):
                carry = lax.optimization_barrier(carry)
            piece = carry["piece"]
            for jb, a in zip(jobs, carry["jobs"]):
                jb[2] = a
            if nxt is not None:
                nxt["st"] = carry["nxt"]
            done = carry["done"]
            t += 1
            if t < len(tiles) and t in firsts and nxt is not None:
                while nxt["s"] <= ring.steps:
                    nxt["st"] = ring.step(nxt["st"], nxt["s"])
                    nxt["s"] += 1
                piece = ring.result(nxt["st"])
                nxt = None

        def assemble(w):
            parts = []
            for h in range(HALVES):
                ids = [i for i, tl in enumerate(tiles) if tl[0] == h and tl[1] == w]
                parts.append(jnp.concatenate([done[i] for i in ids], axis=1))
            x = jnp.stack(parts).reshape(HALVES, group, tc, units)
            return x.transpose(1, 0, 2, 3).reshape(group * HALVES * tc, units)

        gate = assemble(0)
        up = assemble(1)
        return (jax.nn.silu(gate) * up).astype(jnp.bfloat16)

    return on_device


def solution(mesh):
    placed = (P("col", "row"), P("row", "col"), P("row", "col"))
    fn = make_on_device(mesh.shape["row"], mesh.shape["col"], ring_order(mesh))
    return jax.shard_map(
        fn, mesh=mesh, in_specs=placed, out_specs=P("row", "col"), check_vma=False
    )
```

```python
import jax
import jax.numpy as jnp
import numpy as np
from jax import lax
from jax.sharding import PartitionSpec as P

HALVES = 2


def tile_widths(units, last):
    half = units // 2
    if not last:
        return [half, units - half]
    rest = units - half
    small = max(128, (rest // 3) // 128 * 128)
    return [half, rest - small, small]


def ring_order(mesh):
    col = mesh.devices[0]
    n = len(col)
    try:
        zs = sorted({d.coords[2] for d in col})
        xs = sorted({d.coords[0] for d in col})
        at = {(zs.index(d.coords[2]), xs.index(d.coords[0])): i for i, d in enumerate(col)}
    except Exception:
        return list(range(n))
    a, b = len(zs), len(xs)
    if a * b != n or len(at) != n or a % 2 or b < 2:
        return list(range(n))
    cells = [(z, 0) for z in range(a)]
    for k, z in enumerate(range(a - 1, -1, -1)):
        span = range(1, b) if k % 2 == 0 else range(b - 1, 0, -1)
        cells += [(z, x) for x in span]
    return [at[c] for c in cells]


class Ring:
    def __init__(self, order, slot):
        self.slot = slot
        self.order = order
        n = len(order)
        self.n = n
        pos = np.zeros(n, np.int32)
        for q, c in enumerate(order):
            pos[c] = q
        self.pos = pos
        self.fwd_pairs = [(order[q], order[(q + 1) % n]) for q in range(n)]
        self.bwd_pairs = [(order[q], order[(q - 1) % n]) for q in range(n)]
        self.steps = n // 2
        self.back_steps = n - 1 - n // 2

    def init(self, x):
        n = self.n
        c = lax.axis_index("col")
        buf = jnp.zeros((n,) + x.shape, x.dtype)
        buf = lax.dynamic_update_slice(buf, x[None], (self.slot(c), 0, 0))
        p = jnp.asarray(self.pos)[c]
        order_t = jnp.asarray(np.array(self.order, np.int32))
        steps = jnp.arange(n, dtype=jnp.int32)
        fs = self.slot(order_t[(p - steps) % n])
        bs = self.slot(order_t[(p + steps) % n])
        return {"buf": buf, "f": x, "b": x, "fs": fs, "bs": bs}

    def step(self, st, s):
        fs, bs = st["fs"], st["bs"]
        buf = st["buf"]
        b = st["b"]
        if s == self.steps and self.back_steps < s and self.n > 2:
            k2 = b.shape[1] // 2
            f = lax.ppermute(st["f"][:, :k2], "col", self.fwd_pairs)
            b = lax.ppermute(b[:, k2:], "col", self.bwd_pairs)
            src = fs[s]
            buf = lax.dynamic_update_slice(buf, f[None], (src, 0, 0))
            buf = lax.dynamic_update_slice(buf, b[None], (src, 0, k2))
            return {"buf": buf, "f": f, "b": b, "fs": fs, "bs": bs}
        f = lax.ppermute(st["f"], "col", self.fwd_pairs)
        buf = lax.dynamic_update_slice(buf, f[None], (fs[s], 0, 0))
        if s <= self.back_steps:
            b = lax.ppermute(b, "col", self.bwd_pairs)
            buf = lax.dynamic_update_slice(buf, b[None], (bs[s], 0, 0))
        return {"buf": buf, "f": f, "b": b, "fs": fs, "bs": bs}

    def result(self, st):
        buf = st["buf"]
        return buf.reshape((-1,) + buf.shape[2:])


def reduce_level(cur, d, n_row):
    half = cur.shape[0] // 2
    got = lax.ppermute(cur[:half].astype(jnp.bfloat16), "row", [(i, i ^ d) for i in range(n_row)])
    return cur[half:].astype(jnp.float32) + got.astype(jnp.float32)


def target_slot(t, r, n_row):
    x = (t ^ r) ^ (n_row - 1)
    pos = 0
    d, bit = 1, n_row // 2
    while d < n_row:
        pos = pos + ((x // d) % 2) * bit
        d *= 2
        bit //= 2
    return pos


def make_on_device(n_row, n_col, order):
    group = n_col // n_row

    def slot(c):
        r = lax.axis_index("row")
        return target_slot(c // group, r, n_row) * group + c % group

    ring = Ring(order, slot)
    levels = []
    d = 1
    while d < n_row:
        levels.append(d)
        d *= 2

    def on_device(tokens, gate_weight, up_weight):
        local = tokens.shape[0]
        tc = local // HALVES
        group = n_col // n_row
        units = gate_weight.shape[1]

        st = ring.init(tokens[:tc])
        for s in range(1, ring.steps + 1):
            st = ring.step(st, s)
        piece = ring.result(st)
        piece, tokens = lax.optimization_barrier((piece, tokens))

        tiles = []
        for h in range(HALVES):
            for w in range(2):
                start = 0
                for width in tile_widths(units, h == HALVES - 1 and w == 1):
                    tiles.append((h, w, start, width))
                    start += width
        firsts = [i for i, tl in enumerate(tiles) if i == 0 or tl[0] != tiles[i - 1][0]]

        jobs = []
        done = {}
        nxt = None
        t = 0
        while t < len(tiles) or jobs:
            carry = {}
            for job in jobs:
                job[2] = reduce_level(job[2], levels[job[1]], n_row)
                job[1] += 1
            if t < len(tiles):
                h, w, start, width = tiles[t]
                if t in firsts and h + 1 < HALVES:
                    nxt = {"st": ring.init(tokens[(h + 1) * tc:(h + 2) * tc]), "s": 1}
                if nxt is not None and nxt["s"] <= ring.steps:
                    nxt["st"] = ring.step(nxt["st"], nxt["s"])
                    nxt["s"] += 1
                weight = gate_weight if w == 0 else up_weight
                out = jnp.dot(
                    piece, weight[:, start:start + width], preferred_element_type=jnp.float32
                ).astype(jnp.bfloat16)
                new_job = [t, 0, out]
            else:
                new_job = None
            finished = [jb for jb in jobs if jb[1] == len(levels)]
            jobs = [jb for jb in jobs if jb[1] < len(levels)]
            for jb in finished:
                done[jb[0]] = jb[2]
            if new_job is not None:
                if levels:
                    jobs.append(new_job)
                else:
                    done[new_job[0]] = new_job[2].astype(jnp.float32)
            carry["piece"] = piece
            carry["jobs"] = [jb[2] for jb in jobs]
            carry["nxt"] = nxt["st"] if nxt is not None else None
            carry["done"] = done
            if t + 1 < len(tiles):
                carry = lax.optimization_barrier(carry)
            piece = carry["piece"]
            for jb, a in zip(jobs, carry["jobs"]):
                jb[2] = a
            if nxt is not None:
                nxt["st"] = carry["nxt"]
            done = carry["done"]
            t += 1
            if t < len(tiles) and t in firsts and nxt is not None:
                while nxt["s"] <= ring.steps:
                    nxt["st"] = ring.step(nxt["st"], nxt["s"])
                    nxt["s"] += 1
                piece = ring.result(nxt["st"])
                nxt = None

        def assemble(w):
            parts = []
            for h in range(HALVES):
                ids = [i for i, tl in enumerate(tiles) if tl[0] == h and tl[1] == w]
                parts.append(jnp.concatenate([done[i] for i in ids], axis=1))
            x = jnp.stack(parts).reshape(HALVES, group, tc, units)
            return x.transpose(1, 0, 2, 3).reshape(group * HALVES * tc, units)

        gate = assemble(0)
        up = assemble(1)
        return (jax.nn.silu(gate) * up).astype(jnp.bfloat16)

    return on_device


def solution(mesh):
    placed = (P("col", "row"), P("row", "col"), P("row", "col"))
    fn = make_on_device(mesh.shape["row"], mesh.shape["col"], ring_order(mesh))
    return jax.shard_map(
        fn, mesh=mesh, in_specs=placed, out_specs=P("row", "col"), check_vma=False
    )
```

```python
import jax
import jax.numpy as jnp
import numpy as np
from jax import lax
from jax.sharding import PartitionSpec as P

HALVES = 2


def tile_widths(units, last):
    half = units // 2
    if not last:
        return [half, units - half]
    rest = units - half
    small = max(128, (rest // 3) // 128 * 128)
    return [half, rest - small, small]


def ring_order(mesh):
    col = mesh.devices[0]
    n = len(col)
    try:
        zs = sorted({d.coords[2] for d in col})
        xs = sorted({d.coords[0] for d in col})
        at = {(zs.index(d.coords[2]), xs.index(d.coords[0])): i for i, d in enumerate(col)}
    except Exception:
        return list(range(n))
    a, b = len(zs), len(xs)
    if a * b != n or len(at) != n or a % 2 or b < 2:
        return list(range(n))
    cells = [(z, 0) for z in range(a)]
    for k, z in enumerate(range(a - 1, -1, -1)):
        span = range(1, b) if k % 2 == 0 else range(b - 1, 0, -1)
        cells += [(z, x) for x in span]
    return [at[c] for c in cells]


class Ring:
    def __init__(self, order):
        self.order = order
        n = len(order)
        self.n = n
        pos = np.zeros(n, np.int32)
        for q, c in enumerate(order):
            pos[c] = q
        self.pos = pos
        self.fwd_pairs = [(order[q], order[(q + 1) % n]) for q in range(n)]
        self.bwd_pairs = [(order[q], order[(q - 1) % n]) for q in range(n)]
        self.steps = n // 2
        self.back_steps = n - 1 - n // 2

    def init(self, x):
        n = self.n
        c = lax.axis_index("col")
        buf = jnp.zeros((n,) + x.shape, x.dtype)
        buf = lax.dynamic_update_slice(buf, x[None], (c, 0, 0))
        return {"buf": buf, "f": x, "b": x}

    def step(self, st, s):
        n = self.n
        c = lax.axis_index("col")
        p = jnp.asarray(self.pos)[c]
        order_t = jnp.asarray(np.array(self.order, np.int32))
        buf = st["buf"]
        b = st["b"]
        if s == self.steps and self.back_steps < s and n > 2:
            k2 = b.shape[1] // 2
            f = lax.ppermute(st["f"][:, :k2], "col", self.fwd_pairs)
            b = lax.ppermute(b[:, k2:], "col", self.bwd_pairs)
            src = order_t[(p - s) % n]
            buf = lax.dynamic_update_slice(buf, f[None], (src, 0, 0))
            buf = lax.dynamic_update_slice(buf, b[None], (src, 0, k2))
            return {"buf": buf, "f": f, "b": b}
        f = lax.ppermute(st["f"], "col", self.fwd_pairs)
        buf = lax.dynamic_update_slice(buf, f[None], (order_t[(p - s) % n], 0, 0))
        if s <= self.back_steps:
            b = lax.ppermute(b, "col", self.bwd_pairs)
            buf = lax.dynamic_update_slice(buf, b[None], (order_t[(p + s) % n], 0, 0))
        return {"buf": buf, "f": f, "b": b}

    def result(self, st):
        buf = st["buf"]
        return buf.reshape((-1,) + buf.shape[2:])


def reduce_level(cur, d, n_row):
    r = lax.axis_index("row")
    m = cur.shape[0] // (n_row // d)
    x4 = cur.reshape(n_row // (2 * d), 2, m, cur.shape[1])
    bit = (r // d) % 2
    keep = lax.dynamic_index_in_dim(x4, bit, axis=1, keepdims=False)
    send = lax.dynamic_index_in_dim(x4, 1 - bit, axis=1, keepdims=False)
    got = lax.ppermute(send.astype(jnp.bfloat16), "row", [(i, i ^ d) for i in range(n_row)])
    return (keep.astype(jnp.float32) + got.astype(jnp.float32)).reshape(-1, cur.shape[1])


def make_on_device(n_row, n_col, order):
    ring = Ring(order)
    levels = []
    d = 1
    while d < n_row:
        levels.append(d)
        d *= 2

    def on_device(tokens, gate_weight, up_weight):
        local = tokens.shape[0]
        first = (local * 7 // 16) // 8 * 8
        sizes = [first, local - first]
        offs = [0, first]
        group = n_col // n_row
        units = gate_weight.shape[1]

        st = ring.init(tokens[:sizes[0]])
        for s in range(1, ring.steps + 1):
            st = ring.step(st, s)
        piece = ring.result(st)
        piece, tokens = lax.optimization_barrier((piece, tokens))

        tiles = []
        for h in range(HALVES):
            for w in range(2):
                start = 0
                for width in tile_widths(units, h == HALVES - 1 and w == 1):
                    tiles.append((h, w, start, width))
                    start += width
        firsts = [i for i, tl in enumerate(tiles) if i == 0 or tl[0] != tiles[i - 1][0]]

        jobs = []
        done = {}
        nxt = None
        t = 0
        while t < len(tiles) or jobs:
            carry = {}
            for job in jobs:
                job[2] = reduce_level(job[2], levels[job[1]], n_row)
                job[1] += 1
            if t < len(tiles):
                h, w, start, width = tiles[t]
                if t in firsts and h + 1 < HALVES:
                    nxt = {"st": ring.init(tokens[offs[h + 1]:offs[h + 1] + sizes[h + 1]]), "s": 1}
                if nxt is not None and nxt["s"] <= ring.steps:
                    nxt["st"] = ring.step(nxt["st"], nxt["s"])
                    nxt["s"] += 1
                weight = gate_weight if w == 0 else up_weight
                out = jnp.dot(
                    piece, weight[:, start:start + width], preferred_element_type=jnp.float32
                ).astype(jnp.bfloat16)
                new_job = [t, 0, out]
            else:
                new_job = None
            finished = [jb for jb in jobs if jb[1] == len(levels)]
            jobs = [jb for jb in jobs if jb[1] < len(levels)]
            for jb in finished:
                done[jb[0]] = jb[2]
            if new_job is not None:
                if levels:
                    jobs.append(new_job)
                else:
                    done[new_job[0]] = new_job[2].astype(jnp.float32)
            carry["piece"] = piece
            carry["jobs"] = [jb[2] for jb in jobs]
            carry["nxt"] = nxt["st"] if nxt is not None else None
            carry["done"] = done
            if t + 1 < len(tiles):
                carry = lax.optimization_barrier(carry)
            piece = carry["piece"]
            for jb, a in zip(jobs, carry["jobs"]):
                jb[2] = a
            if nxt is not None:
                nxt["st"] = carry["nxt"]
            done = carry["done"]
            t += 1
            if t < len(tiles) and t in firsts and nxt is not None:
                while nxt["s"] <= ring.steps:
                    nxt["st"] = ring.step(nxt["st"], nxt["s"])
                    nxt["s"] += 1
                piece = ring.result(nxt["st"])
                nxt = None

        def assemble(w):
            parts = []
            for h in range(HALVES):
                ids = [i for i, tl in enumerate(tiles) if tl[0] == h and tl[1] == w]
                parts.append(jnp.concatenate([done[i] for i in ids], axis=1))
            parts = [x.reshape(group, sizes[h], units) for h, x in enumerate(parts)]
            return jnp.concatenate(parts, axis=1).reshape(group * local, units)

        gate = assemble(0)
        up = assemble(1)
        return (jax.nn.silu(gate) * up).astype(jnp.bfloat16)

    return on_device


def solution(mesh):
    placed = (P("col", "row"), P("row", "col"), P("row", "col"))
    fn = make_on_device(mesh.shape["row"], mesh.shape["col"], ring_order(mesh))
    return jax.shard_map(
        fn, mesh=mesh, in_specs=placed, out_specs=P("row", "col"), check_vma=False
    )
```

```python
import jax
import jax.numpy as jnp
import numpy as np
from jax import lax
from jax.sharding import PartitionSpec as P

HALVES = 2


def tile_widths(units, last):
    half = units // 2
    if not last:
        return [half, units - half]
    rest = units - half
    small = max(128, (rest // 3) // 128 * 128)
    return [half, rest - small, small]


def ring_order(mesh):
    col = mesh.devices[0]
    n = len(col)
    try:
        zs = sorted({d.coords[2] for d in col})
        xs = sorted({d.coords[0] for d in col})
        at = {(zs.index(d.coords[2]), xs.index(d.coords[0])): i for i, d in enumerate(col)}
    except Exception:
        return list(range(n))
    a, b = len(zs), len(xs)
    if a * b != n or len(at) != n or a % 2 or b < 2:
        return list(range(n))
    cells = [(z, 0) for z in range(a)]
    for k, z in enumerate(range(a - 1, -1, -1)):
        span = range(1, b) if k % 2 == 0 else range(b - 1, 0, -1)
        cells += [(z, x) for x in span]
    return [at[c] for c in cells]


class Ring:
    def __init__(self, order):
        self.order = order
        n = len(order)
        self.n = n
        pos = np.zeros(n, np.int32)
        for q, c in enumerate(order):
            pos[c] = q
        self.pos = pos
        self.fwd_pairs = [(order[q], order[(q + 1) % n]) for q in range(n)]
        self.bwd_pairs = [(order[q], order[(q - 1) % n]) for q in range(n)]
        self.steps = n // 2
        self.back_steps = n - 1 - n // 2

    def init(self, x):
        n = self.n
        c = lax.axis_index("col")
        buf = jnp.zeros((n,) + x.shape, x.dtype)
        buf = lax.dynamic_update_slice(buf, x[None], (c, 0, 0))
        return {"buf": buf, "f": x, "b": x}

    def step(self, st, s):
        n = self.n
        c = lax.axis_index("col")
        p = jnp.asarray(self.pos)[c]
        order_t = jnp.asarray(np.array(self.order, np.int32))
        buf = st["buf"]
        b = st["b"]
        if s == self.steps and self.back_steps < s and n > 2:
            k2 = b.shape[1] // 2
            f = lax.ppermute(st["f"][:, :k2], "col", self.fwd_pairs)
            b = lax.ppermute(b[:, k2:], "col", self.bwd_pairs)
            src = order_t[(p - s) % n]
            buf = lax.dynamic_update_slice(buf, f[None], (src, 0, 0))
            buf = lax.dynamic_update_slice(buf, b[None], (src, 0, k2))
            return {"buf": buf, "f": f, "b": b}
        f = lax.ppermute(st["f"], "col", self.fwd_pairs)
        buf = lax.dynamic_update_slice(buf, f[None], (order_t[(p - s) % n], 0, 0))
        if s <= self.back_steps:
            b = lax.ppermute(b, "col", self.bwd_pairs)
            buf = lax.dynamic_update_slice(buf, b[None], (order_t[(p + s) % n], 0, 0))
        return {"buf": buf, "f": f, "b": b}

    def result(self, st):
        buf = st["buf"]
        return buf.reshape((-1,) + buf.shape[2:])


def reduce_level(cur, d, n_row):
    r = lax.axis_index("row")
    m = cur.shape[0] // (n_row // d)
    x4 = cur.reshape(n_row // (2 * d), 2, m, cur.shape[1])
    bit = (r // d) % 2
    keep = lax.dynamic_index_in_dim(x4, bit, axis=1, keepdims=False)
    send = lax.dynamic_index_in_dim(x4, 1 - bit, axis=1, keepdims=False)
    got = lax.ppermute(send.astype(jnp.bfloat16), "row", [(i, i ^ d) for i in range(n_row)])
    return (keep.astype(jnp.float32) + got.astype(jnp.float32)).reshape(-1, cur.shape[1])


def make_on_device(n_row, n_col, order):
    ring = Ring(order)
    levels = []
    d = 1
    while d < n_row:
        levels.append(d)
        d *= 2

    def on_device(tokens, gate_weight, up_weight):
        local = tokens.shape[0]
        first = (local * 9 // 16) // 8 * 8
        sizes = [first, local - first]
        offs = [0, first]
        group = n_col // n_row
        units = gate_weight.shape[1]

        st = ring.init(tokens[:sizes[0]])
        for s in range(1, ring.steps + 1):
            st = ring.step(st, s)
        piece = ring.result(st)
        piece, tokens = lax.optimization_barrier((piece, tokens))

        tiles = []
        for h in range(HALVES):
            for w in range(2):
                start = 0
                for width in tile_widths(units, h == HALVES - 1 and w == 1):
                    tiles.append((h, w, start, width))
                    start += width
        firsts = [i for i, tl in enumerate(tiles) if i == 0 or tl[0] != tiles[i - 1][0]]

        jobs = []
        done = {}
        nxt = None
        t = 0
        while t < len(tiles) or jobs:
            carry = {}
            for job in jobs:
                job[2] = reduce_level(job[2], levels[job[1]], n_row)
                job[1] += 1
            if t < len(tiles):
                h, w, start, width = tiles[t]
                if t in firsts and h + 1 < HALVES:
                    nxt = {"st": ring.init(tokens[offs[h + 1]:offs[h + 1] + sizes[h + 1]]), "s": 1}
                if nxt is not None and nxt["s"] <= ring.steps:
                    nxt["st"] = ring.step(nxt["st"], nxt["s"])
                    nxt["s"] += 1
                weight = gate_weight if w == 0 else up_weight
                out = jnp.dot(
                    piece, weight[:, start:start + width], preferred_element_type=jnp.float32
                ).astype(jnp.bfloat16)
                new_job = [t, 0, out]
            else:
                new_job = None
            finished = [jb for jb in jobs if jb[1] == len(levels)]
            jobs = [jb for jb in jobs if jb[1] < len(levels)]
            for jb in finished:
                done[jb[0]] = jb[2]
            if new_job is not None:
                if levels:
                    jobs.append(new_job)
                else:
                    done[new_job[0]] = new_job[2].astype(jnp.float32)
            carry["piece"] = piece
            carry["jobs"] = [jb[2] for jb in jobs]
            carry["nxt"] = nxt["st"] if nxt is not None else None
            carry["done"] = done
            if t + 1 < len(tiles):
                carry = lax.optimization_barrier(carry)
            piece = carry["piece"]
            for jb, a in zip(jobs, carry["jobs"]):
                jb[2] = a
            if nxt is not None:
                nxt["st"] = carry["nxt"]
            done = carry["done"]
            t += 1
            if t < len(tiles) and t in firsts and nxt is not None:
                while nxt["s"] <= ring.steps:
                    nxt["st"] = ring.step(nxt["st"], nxt["s"])
                    nxt["s"] += 1
                piece = ring.result(nxt["st"])
                nxt = None

        def assemble(w):
            parts = []
            for h in range(HALVES):
                ids = [i for i, tl in enumerate(tiles) if tl[0] == h and tl[1] == w]
                parts.append(jnp.concatenate([done[i] for i in ids], axis=1))
            parts = [x.reshape(group, sizes[h], units) for h, x in enumerate(parts)]
            return jnp.concatenate(parts, axis=1).reshape(group * local, units)

        gate = assemble(0)
        up = assemble(1)
        return (jax.nn.silu(gate) * up).astype(jnp.bfloat16)

    return on_device


def solution(mesh):
    placed = (P("col", "row"), P("row", "col"), P("row", "col"))
    fn = make_on_device(mesh.shape["row"], mesh.shape["col"], ring_order(mesh))
    return jax.shard_map(
        fn, mesh=mesh, in_specs=placed, out_specs=P("row", "col"), check_vma=False
    )
```
